512 devices in a mesh: req: 16 (over z), tp: 32 (over x, y, core).
Axes of the slice: x: 4, y: 4, z: 16, core: 2. Of those that a mesh axis runs over, the one named last changes fastest.
Arguments:
- hidden: bfloat16 [1024, 5120], P(('req', 'tp')), may hold values from -6 to 6
- input_norm_gain: float32 [5120], replicated, may hold values from 0.1 to 1.9
- query_weight: bfloat16 [5120, 4096], P(None, 'tp'), may hold values from -1 to 1
- key_weight: bfloat16 [128, 8, 5120], P('tp'), may hold values from -0.078125 to 0.078125
- value_weight: bfloat16 [128, 8, 5120], P('tp'), may hold values from -0.078125 to 0.078125
- output_weight: bfloat16 [4096, 5120], P('tp'), may hold values from -0.09375 to 0.09375
- query_bias_vector: float32 [4096], P('tp'), may hold values from -3 to 3
- value_bias_vector: float32 [128, 8], P('tp'), may hold values from -3 to 3
- adapter_down_maps: bfloat16 [16, 5120, 32], P('req', 'tp'), may hold values from -0.078125 to 0.078125
- adapter_query_up: bfloat16 [16, 16, 4096], P('req', None, 'tp'), may hold values from -1.5 to 1.5
- adapter_value_up: bfloat16 [16, 16, 128, 8], P('req', None, 'tp'), may hold values from -1.5 to 1.5
- lengths: int32 [16, 8], P('req'), may hold values from 1 to 32, 64 in all within a row
- prompt_adapter: int32 [16, 8], P('req'), may hold values from 0 to 15
Outputs:
- output: bfloat16 [1024, 5120], P(('req', 'tp'))
The draws below stay inside these ranges and needn't reach their ends.
All inputs are finite; a program needn't handle non-finite values.
Results may differ from the reference program's by a relative error of at most 0.019.
Values may be sent and summed in bfloat16 or wider, within the bound.
No kernel may reach another device: no remote copies, remote signals or barrier semaphores. Data moves between devices by JAX's collectives and lax.ppermute only.
A program may use at most 128 MiB of HBM per device.

```python
import math
import jax
import jax.numpy as jnp
import numpy as np
from jax import lax

MODEL_WIDTH = 5120
HD = 128
HK = 8
HQ = 32
ADAPTER_RANK = 16
SEQS = 8
QUERY_FEATURES = 4096
KEY_FEATURES = 1024
HPD = 1
ADAPTER_COUNT = 16
GTOK = 64
TOKENS = 1024
N_REQ = 16
N_TP = 32


def draw_query_weight(key, part):
    first_key = jax.random.fold_in(jax.random.fold_in(key, 11), 0)
    base_values = jnp.clip(jax.random.normal(first_key, (MODEL_WIDTH, QUERY_FEATURES), jnp.float32), -6.0, 6.0)
    return (base_values * MODEL_WIDTH ** (-0.5)).astype(jnp.bfloat16)


def plant(array, stream_key, low, largest):
    spot = [jax.random.randint(jax.random.fold_in(stream_key, axis), (), 0, length) for axis, length in enumerate(array.shape)]
    main_axis = array.shape.index(max(array.shape))
    next_to = spot[:main_axis] + [(spot[main_axis] + 1) % array.shape[main_axis]] + spot[main_axis + 1:]
    return array.at[tuple(spot)].set(low).at[tuple(next_to)].set(largest)


def level_of(own_key, dims, pieces, least, largest):
    gain = 1.0
    for position, parts in pieces:
        steps = jax.random.uniform(jax.random.fold_in(jax.random.fold_in(own_key, 6), position), (parts,), jnp.float32, least / len(pieces), largest / len(pieces))
        gain = gain * jnp.repeat(jnp.exp(steps), dims[position] // parts).reshape((-1,) + (1,) * (len(dims) - 1 - position))
    return gain


def profile(number_of, total, limit, slope):
    weights = [(1 << 20) // math.isqrt(grade ** slope) + 1 for grade in range(2, number_of + 1)]
    spare, counts = total - limit - (number_of - 1), [1] * (number_of - 1)
    while spare > 0:
        free = [i for i in range(number_of - 1) if counts[i] < limit]
        mass, budget = sum([weights[i] for i in free]), spare
        for i in free:
            extra = min(limit - counts[i], max(1, budget * weights[i] // mass), spare)
            counts[i] = counts[i] + extra
            spare = spare - extra
    return np.array([limit] + counts)


def uneven_parts(stream_key, count, total, bound, slope):
    if count == 2:
        one = jax.random.randint(stream_key, (), max(1, total - bound), min(bound, total - 1) + 1)
        return jnp.stack([one, total - one])
    sizes = jnp.asarray(profile(count, total, bound, slope), jnp.int32)
    couples = (count - 1) // 2
    giver, sink = sizes[1:1 + 2 * couples:2], sizes[2:2 + 2 * couples:2]
    margin = jnp.minimum(giver - 1, bound - sink)
    shifted = jax.random.randint(jax.random.fold_in(stream_key, 1), (couples,), 0, 1 << 20) % (margin + 1)
    sizes = sizes.at[1:1 + 2 * couples:2].set(giver - shifted).at[2:2 + 2 * couples:2].set(sink + shifted)
    return sizes[jax.random.permutation(jax.random.fold_in(stream_key, 2), count)]


def normal_values(key, extent, scale, most, cuts=(), kind=jnp.bfloat16):
    values = jax.random.normal(key, extent, jnp.float32) * scale
    if len(cuts) > 0:
        values = level_of(key, extent, cuts, -0.22, 0.18) * values
    return jnp.clip(values, min=-most, max=most).astype(kind)


def setup_inputs(seed: int = 0) -> dict:
    arg_keys = jax.random.split(jax.random.key(seed), 14)
    hidden = normal_values(arg_keys[0], (TOKENS, MODEL_WIDTH), 1.0, 6.0, ((0, 512),))
    input_norm_gain = jnp.clip(1.0 + 0.18 * jax.random.normal(arg_keys[1], (MODEL_WIDTH,), jnp.float32), 0.1, 1.9)
    query_weight = draw_query_weight(jax.random.fold_in(arg_keys[13], 71), 0)
    key_weight = normal_values(arg_keys[3], (HD, HK, MODEL_WIDTH), MODEL_WIDTH ** -0.5, 0.078125, ((0, 32),))
    value_weight = normal_values(arg_keys[4], (HD, HK, MODEL_WIDTH), MODEL_WIDTH ** -0.5, 0.078125, ((0, 32),))
    output_weight = normal_values(arg_keys[5], (QUERY_FEATURES, MODEL_WIDTH), QUERY_FEATURES ** -0.5, 0.09375, ((0, 32),))
    query_bias_vector = normal_values(arg_keys[6], (QUERY_FEATURES,), 0.5, 3.0, ((0, 32),), jnp.float32)
    value_bias_vector = normal_values(arg_keys[7], (HD, HK), 0.5, 3.0, ((0, 32),), jnp.float32)
    adapter_down_maps = normal_values(arg_keys[8], (ADAPTER_COUNT, MODEL_WIDTH, 2 * ADAPTER_RANK), MODEL_WIDTH ** -0.5, 0.078125, ((0, 16), (1, 32)))
    adapter_query_up = normal_values(arg_keys[9], (ADAPTER_COUNT, ADAPTER_RANK, QUERY_FEATURES), ADAPTER_RANK ** -0.5, 1.5, ((0, 16), (2, 32)))
    adapter_value_up = normal_values(arg_keys[10], (ADAPTER_COUNT, ADAPTER_RANK, HD, HK), ADAPTER_RANK ** -0.5, 1.5, ((0, 16), (2, 32)))
    lengths = jax.vmap(lambda own: uneven_parts(own, SEQS, GTOK, GTOK // 2, 2))(jax.random.split(arg_keys[11], N_REQ)).reshape((N_REQ, SEQS)).astype(jnp.int32)
    prompt_adapter = plant(jax.random.randint(arg_keys[12], (N_REQ, SEQS), 0, ADAPTER_COUNT), jax.random.fold_in(arg_keys[12], 1), 0, ADAPTER_COUNT - 1).astype(jnp.int32)
    return dict(hidden=hidden, input_norm_gain=input_norm_gain, query_weight=query_weight, key_weight=key_weight, value_weight=value_weight, output_weight=output_weight, query_bias_vector=query_bias_vector, value_bias_vector=value_bias_vector, adapter_down_maps=adapter_down_maps, adapter_query_up=adapter_query_up, adapter_value_up=adapter_value_up, lengths=lengths, prompt_adapter=prompt_adapter)


eps = 1e-06
rope_base = 1000000.0

def prompt_layout(prompt_length_list, group_tokens):
    ends = jnp.cumsum(prompt_length_list).astype(jnp.int32)
    starts = (ends - prompt_length_list).astype(jnp.int32)
    places = jnp.arange(group_tokens, dtype=jnp.int32)
    group_entry = (places[:, None] >= starts[None, :]) & (places[:, None] < ends[None, :])
    chosen = group_entry.astype(jnp.int32)
    segment = lax.optimization_barrier(jnp.sum(chosen * jnp.arange(prompt_length_list.shape[0], dtype=jnp.int32)[None, :], axis=1)).astype(jnp.int32)
    offset = (places - lax.optimization_barrier(jnp.sum(chosen * starts[None, :], axis=1))).astype(jnp.int32)
    return (group_entry, segment, offset)

def rotate(values, offset):
    width = values.shape[-1]
    half_width = width // 2
    frequency = rope_base ** (-(jnp.arange(half_width, dtype=jnp.float32) * 2.0) / width)
    angles = offset.astype(jnp.float32)[:, None] * frequency[None, :]
    cosine = jnp.cos(angles)[:, None, :]
    sines = jnp.sin(angles)[:, None, :]
    lower_half = values[..., :half_width]
    upper_half = values[..., half_width:]
    return jnp.concatenate([lower_half * cosine - upper_half * sines, upper_half * cosine + lower_half * sines], axis=-1)

def reduced_rank_term(hidden_code, group_entry, table):
    row_count = hidden_code.shape[0]
    spread = jnp.where(group_entry[:, :, None], hidden_code[:, None, :], jnp.zeros((), jnp.bfloat16))
    return jnp.dot(spread.reshape(row_count, -1), table.reshape(-1, table.shape[-1]), preferred_element_type=jnp.float32)

def single_group(hidden, prompt_length_list, adapter_choice_list, input_norm_gain, query_weight, key_weight, value_weight, output_weight, query_bias_vector, value_bias_vector, adapter_down_maps, adapter_query_up, adapter_value_up):
    group_entry, segment, offset = prompt_layout(prompt_length_list, GTOK)
    values = hidden.astype(jnp.float32)
    normalized_input = (values * lax.rsqrt(lax.optimization_barrier(jnp.mean(values * values, axis=-1, keepdims=True)) + eps) * input_norm_gain).astype(jnp.bfloat16)
    reduced_rows = adapter_down_maps[adapter_choice_list].astype(jnp.float32)
    terms = jnp.einsum('td,sdr->tsr', normalized_input.astype(jnp.float32), reduced_rows)
    hidden_code = lax.optimization_barrier(jnp.sum(jnp.where(group_entry[:, :, None], terms, jnp.float32(0.0)), axis=1)).astype(jnp.bfloat16)
    query_rows = jnp.dot(normalized_input, query_weight, preferred_element_type=jnp.float32) + query_bias_vector + reduced_rank_term(hidden_code[:, :ADAPTER_RANK], group_entry, adapter_query_up[adapter_choice_list])
    key_proj = jnp.dot(normalized_input, key_weight.T, preferred_element_type=jnp.float32).astype(jnp.bfloat16)
    value_matrix_rows = (jnp.dot(normalized_input, value_weight.T, preferred_element_type=jnp.float32) + value_bias_vector + reduced_rank_term(hidden_code[:, ADAPTER_RANK:], group_entry, adapter_value_up[adapter_choice_list])).astype(jnp.bfloat16)
    query_rot = rotate(query_rows.reshape(GTOK, HQ, HD), offset).astype(jnp.bfloat16)
    key_rot = rotate(key_proj.astype(jnp.float32).reshape(GTOK, HK, HD), offset).astype(jnp.bfloat16)
    group_size = HQ // HK
    key_full = jnp.repeat(key_rot, group_size, axis=1).astype(jnp.float32)
    value_full = jnp.repeat(value_matrix_rows.reshape(GTOK, HK, HD), group_size, axis=1).astype(jnp.float32)
    scores = jnp.einsum('qhd,khd->hqk', query_rot.astype(jnp.float32), key_full) * HD ** (-0.5)
    places = jnp.arange(GTOK, dtype=jnp.int32)
    allowed = (segment[:, None] == segment[None, :]) & (places[None, :] <= places[:, None])
    scores = jnp.where(allowed[None], scores, jnp.float32(-1e+30))
    row_max = lax.optimization_barrier(jnp.max(scores, axis=-1, keepdims=True))
    weights = jnp.exp(scores - row_max)
    probabilities = (weights / lax.optimization_barrier(jnp.sum(weights, axis=-1, keepdims=True))).astype(jnp.bfloat16)
    mixed = jnp.einsum('hqk,khd->qhd', probabilities.astype(jnp.float32), value_full).astype(jnp.bfloat16).reshape(GTOK, QUERY_FEATURES)
    block_width = HPD * HD
    mixed_blocks = mixed.reshape(GTOK, N_TP, block_width)
    weight_blocks = output_weight.reshape(N_TP, block_width, MODEL_WIDTH)

    def add_block(block_index, total):
        block_rows = lax.dynamic_index_in_dim(mixed_blocks, block_index, 1, keepdims=False)
        block_weight = lax.dynamic_index_in_dim(weight_blocks, block_index, 0, keepdims=False)
        block_term = jnp.dot(block_rows, block_weight, preferred_element_type=jnp.float32).astype(jnp.bfloat16)
        block_term = lax.optimization_barrier(block_term)
        return total + block_term.astype(jnp.float32)
    projected = lax.fori_loop(0, N_TP, add_block, jnp.zeros((GTOK, MODEL_WIDTH), jnp.float32))
    return (values + projected).astype(jnp.bfloat16)

def reference(hidden, input_norm_gain, query_weight, key_weight, value_weight, output_weight, query_bias_vector, value_bias_vector, adapter_down_maps, adapter_query_up, adapter_value_up, lengths, prompt_adapter):
    grouped = hidden.reshape(N_REQ, GTOK, MODEL_WIDTH)
    key_flat = jnp.transpose(key_weight, (1, 0, 2)).reshape(KEY_FEATURES, MODEL_WIDTH)
    value_flat = jnp.transpose(value_weight, (1, 0, 2)).reshape(KEY_FEATURES, MODEL_WIDTH)
    value_bias_flat = jnp.transpose(value_bias_vector, (1, 0)).reshape(KEY_FEATURES)
    value_up_flat = jnp.transpose(adapter_value_up, (0, 1, 3, 2)).reshape(ADAPTER_COUNT, ADAPTER_RANK, KEY_FEATURES)

    def run_group(packed_prompt):
        return single_group(packed_prompt[0], packed_prompt[1], packed_prompt[2], input_norm_gain, query_weight, key_flat, value_flat, output_weight, query_bias_vector, value_bias_flat, adapter_down_maps, adapter_query_up, value_up_flat)
    return lax.map(run_group, (grouped, lengths, prompt_adapter)).reshape(TOKENS, MODEL_WIDTH)
```

```python
import jax
import jax.numpy as jnp
from jax import lax
from jax.sharding import PartitionSpec as P

HD = 128
HK = 8
HQ = 32


eps = 1e-06
rope_base = 1000000.0


def prompt_layout(prompt_length_list, group_tokens):
    ends = jnp.cumsum(prompt_length_list)
    starts = ends - prompt_length_list
    places = jnp.arange(group_tokens, dtype=jnp.int32)
    group_entry = (places[:, None] >= starts[None, :]) & (places[:, None] < ends[None, :])
    chosen = group_entry.astype(jnp.int32)
    segment = jnp.sum(
        chosen * jnp.arange(prompt_length_list.shape[0], dtype=jnp.int32)[None, :], axis=1
    )
    offset = places - jnp.sum(chosen * starts[None, :], axis=1)
    return (group_entry, segment, offset)


def rms_rows(source, input_norm_gain):
    values = source.astype(jnp.float32)
    return (
        values
        * lax.rsqrt(jnp.mean(values * values, axis=-1, keepdims=True) + eps)
        * input_norm_gain
    ).astype(jnp.bfloat16)


def rotate(values, offset):
    width = values.shape[-1]
    half_width = width // 2
    frequency = rope_base ** (-(jnp.arange(half_width, dtype=jnp.float32) * 2.0) / width)
    angles = offset.astype(jnp.float32)[:, None] * frequency[None, :]
    cosine = jnp.cos(angles)[:, None, :]
    sines = jnp.sin(angles)[:, None, :]
    lower_half = values[..., :half_width]
    upper_half = values[..., half_width:]
    return jnp.concatenate(
        [lower_half * cosine - upper_half * sines, upper_half * cosine + lower_half * sines],
        axis=-1,
    )


def attend(query_rot, key_rot, value_head, segment):
    scores = jnp.einsum(
        "qhd,kd->hqk", query_rot, key_rot, preferred_element_type=jnp.float32
    ) * HD ** (-0.5)
    places = jnp.arange(segment.shape[0], dtype=jnp.int32)
    allowed = (segment[:, None] == segment[None, :]) & (places[None, :] <= places[:, None])
    scores = jnp.where(allowed[None], scores, jnp.float32(-1e30))
    row_max = jnp.max(scores, axis=-1, keepdims=True)
    weights = jnp.exp(scores - row_max)
    probabilities = (weights / jnp.sum(weights, axis=-1, keepdims=True)).astype(jnp.bfloat16)
    mixed = jnp.einsum("hqk,kd->qhd", probabilities, value_head, preferred_element_type=jnp.float32)
    return mixed.astype(jnp.bfloat16)


def shards(
    hidden,
    input_norm_gain,
    query_weight,
    key_weight,
    value_weight,
    output_weight,
    query_bias_vector,
    value_bias_vector,
    adapter_down_maps,
    adapter_query_up,
    adapter_value_up,
    lengths,
    prompt_adapter,
):
    tp_width = lax.axis_size("tp")
    tp_place = lax.axis_index("tp")
    tok_rows = hidden.shape[0]
    group_tokens = tok_rows * tp_width
    rank_extent = adapter_query_up.shape[1]
    entry_slice = key_weight.shape[0]
    kv_heads = key_weight.shape[1]
    feat_slice = adapter_down_maps.shape[1]
    head_count = query_weight.shape[1] // HD

    down_flat = adapter_down_maps.reshape(1, -1)
    query_flat = adapter_query_up.reshape(1, -1)
    value_flat = adapter_value_up.reshape(1, -1)
    bank = lax.all_gather(
        jnp.concatenate([down_flat, query_flat, value_flat], axis=1), "req", axis=0, tiled=True
    )
    adapter_total = bank.shape[0]
    n_down, n_query = down_flat.shape[1], query_flat.shape[1]
    bank_down = bank[:, :n_down].reshape((adapter_total,) + adapter_down_maps.shape[1:])
    bank_query = bank[:, n_down : n_down + n_query].reshape(
        (adapter_total,) + adapter_query_up.shape[1:]
    )
    bank_value = bank[:, n_down + n_query :].reshape((adapter_total,) + adapter_value_up.shape[1:])

    prompt_length_list = lengths[0]
    adapter_choice_list = prompt_adapter[0]
    group_entry, segment, offset = prompt_layout(prompt_length_list, group_tokens)
    token_adapter = jnp.take(adapter_choice_list, segment)
    adapter_pick = token_adapter[:, None] == jnp.arange(adapter_total, dtype=jnp.int32)[None, :]

    gathered = lax.all_gather(hidden, "tp", axis=0, tiled=True)
    normalized_input = rms_rows(gathered, input_norm_gain)

    own_features = lax.dynamic_slice_in_dim(
        normalized_input, tp_place * feat_slice, feat_slice, 1
    )
    terms = jnp.einsum(
        "tf,afr->tar", own_features, bank_down, preferred_element_type=jnp.float32
    )
    latent_part = jnp.sum(jnp.where(adapter_pick[:, :, None], terms, 0.0), axis=1)

    key_cols = jnp.einsum(
        "tm,ehm->the", normalized_input, key_weight, preferred_element_type=jnp.float32
    )
    value_cols = (
        jnp.einsum(
            "tm,ehm->the", normalized_input, value_weight, preferred_element_type=jnp.float32
        )
        + jnp.transpose(value_bias_vector)[None, :, :]
    )
    dest = jnp.arange(tp_width, dtype=jnp.int32)
    dest_head = dest * head_count // (HQ // HK)
    key_send = jnp.take(key_cols, dest_head, axis=1).transpose(1, 0, 2).reshape(tp_width, -1)
    value_send = jnp.take(value_cols, dest_head, axis=1).transpose(1, 0, 2).reshape(tp_width, -1)
    latent_send = jnp.broadcast_to(latent_part.reshape(1, -1), (tp_width, latent_part.size))
    up_send = (
        jnp.take(bank_value, dest_head, axis=3)
        .astype(jnp.float32)
        .transpose(3, 0, 1, 2)
        .reshape(tp_width, -1)
    )
    n_key, n_value, n_latent = key_send.shape[1], value_send.shape[1], latent_send.shape[1]
    received = lax.all_to_all(
        jnp.concatenate([key_send, value_send, latent_send, up_send], axis=1),
        "tp",
        0,
        0,
        tiled=True,
    )
    key_head = (
        received[:, :n_key]
        .reshape(tp_width, group_tokens, entry_slice)
        .transpose(1, 0, 2)
        .reshape(group_tokens, HD)
        .astype(jnp.bfloat16)
    )
    value_base = (
        received[:, n_key : n_key + n_value]
        .reshape(tp_width, group_tokens, entry_slice)
        .transpose(1, 0, 2)
        .reshape(group_tokens, HD)
    )
    latent = (
        jnp.sum(
            received[:, n_key + n_value : n_key + n_value + n_latent].reshape(
                tp_width, group_tokens, 2 * rank_extent
            ),
            axis=0,
        )
        .astype(jnp.bfloat16)
    )
    value_up_head = (
        received[:, n_key + n_value + n_latent :]
        .reshape(tp_width, adapter_total, rank_extent, entry_slice)
        .transpose(1, 2, 0, 3)
        .reshape(adapter_total, rank_extent, HD)
    )

    pick = adapter_pick.astype(jnp.bfloat16)
    query_latent = (latent[:, None, :rank_extent] * pick[:, :, None]).reshape(group_tokens, -1)
    value_latent = (latent[:, None, rank_extent:] * pick[:, :, None]).reshape(group_tokens, -1)
    query_rows = (
        jnp.dot(normalized_input, query_weight, preferred_element_type=jnp.float32)
        + query_bias_vector
        + jnp.dot(
            query_latent,
            bank_query.reshape(-1, bank_query.shape[-1]),
            preferred_element_type=jnp.float32,
        )
    )
    value_head = (
        value_base
        + jnp.dot(
            value_latent,
            value_up_head.astype(jnp.bfloat16).reshape(-1, HD),
            preferred_element_type=jnp.float32,
        )
    ).astype(jnp.bfloat16)

    key_rot = rotate(key_head.astype(jnp.float32).reshape(group_tokens, 1, HD), offset)[
        :, 0, :
    ].astype(jnp.bfloat16)
    query_rot = rotate(query_rows.reshape(group_tokens, head_count, HD), offset).astype(
        jnp.bfloat16
    )
    mixed_heads = attend(query_rot, key_rot, value_head, segment).reshape(
        group_tokens, head_count * HD
    )
    block_terms = jnp.dot(mixed_heads, output_weight, preferred_element_type=jnp.float32).astype(
        jnp.bfloat16
    )
    owner_terms = lax.all_to_all(
        block_terms.reshape(tp_width, tok_rows, block_terms.shape[-1]), "tp", 0, 0, tiled=True
    )
    projected = jnp.sum(owner_terms.astype(jnp.float32), axis=0)
    return (hidden.astype(jnp.float32) + projected).astype(jnp.bfloat16)


def solution(mesh):
    return jax.shard_map(
        shards,
        mesh=mesh,
        in_specs=(
            P(("req", "tp"), None),
            P(),
            P(None, "tp"),
            P("tp", None, None),
            P("tp", None, None),
            P("tp", None),
            P("tp"),
            P("tp", None),
            P("req", "tp", None),
            P("req", None, "tp"),
            P("req", None, "tp", None),
            P("req", None),
            P("req", None),
        ),
        out_specs=P(("req", "tp"), None),
        check_vma=False,
    )
```

```python
import jax
import jax.numpy as jnp
from jax import lax
from jax.sharding import PartitionSpec as P

HD = 128
HK = 8
HQ = 32


eps = 1e-06
rope_base = 1000000.0


def prompt_layout(prompt_length_list, group_tokens):
    ends = jnp.cumsum(prompt_length_list)
    starts = ends - prompt_length_list
    places = jnp.arange(group_tokens, dtype=jnp.int32)
    group_entry = (places[:, None] >= starts[None, :]) & (places[:, None] < ends[None, :])
    chosen = group_entry.astype(jnp.int32)
    segment = jnp.sum(
        chosen * jnp.arange(prompt_length_list.shape[0], dtype=jnp.int32)[None, :], axis=1
    )
    offset = places - jnp.sum(chosen * starts[None, :], axis=1)
    return (group_entry, segment, offset)


def rms_rows(source, input_norm_gain):
    values = source.astype(jnp.float32)
    return (
        values
        * lax.rsqrt(jnp.mean(values * values, axis=-1, keepdims=True) + eps)
        * input_norm_gain
    ).astype(jnp.bfloat16)


def rotate(values, offset):
    width = values.shape[-1]
    half_width = width // 2
    frequency = rope_base ** (-(jnp.arange(half_width, dtype=jnp.float32) * 2.0) / width)
    angles = offset.astype(jnp.float32)[:, None] * frequency[None, :]
    cosine = jnp.cos(angles)[:, None, :]
    sines = jnp.sin(angles)[:, None, :]
    lower_half = values[..., :half_width]
    upper_half = values[..., half_width:]
    return jnp.concatenate(
        [lower_half * cosine - upper_half * sines, upper_half * cosine + lower_half * sines],
        axis=-1,
    )


def ring_gather(x, axis, n):
    parts = [x] + [lax.ppermute(x, axis, [(i, (i - k) % n) for i in range(n)]) for k in range(1, n)]
    rel = jnp.stack(parts)
    me = lax.axis_index(axis)
    return lax.dynamic_slice_in_dim(jnp.concatenate([rel, rel]), n - me, n, 0)


def ring_deliver(send, axis, n):
    me = lax.axis_index(axis)
    rot = lax.dynamic_slice_in_dim(jnp.concatenate([send, send]), me, n, 0)
    parts = [rot[0]] + [
        lax.ppermute(rot[k], axis, [(i, (i + k) % n) for i in range(n)]) for k in range(1, n)
    ]
    return jnp.stack(parts)


def source_order(rel, axis, n):
    me = lax.axis_index(axis)
    both = jnp.concatenate([rel, rel])
    return jnp.flip(lax.dynamic_slice_in_dim(both, me + 1, n, 0), axis=0)


def attend(query_rot, key_rot, value_head, segment):
    scores = jnp.einsum(
        "qhd,kd->hqk", query_rot, key_rot, preferred_element_type=jnp.float32
    ) * HD ** (-0.5)
    places = jnp.arange(segment.shape[0], dtype=jnp.int32)
    allowed = (segment[:, None] == segment[None, :]) & (places[None, :] <= places[:, None])
    scores = jnp.where(allowed[None], scores, jnp.float32(-1e30))
    row_max = jnp.max(scores, axis=-1, keepdims=True)
    weights = jnp.exp(scores - row_max)
    probabilities = (weights / jnp.sum(weights, axis=-1, keepdims=True)).astype(jnp.bfloat16)
    mixed = jnp.einsum("hqk,kd->qhd", probabilities, value_head, preferred_element_type=jnp.float32)
    return mixed.astype(jnp.bfloat16)


def shards(
    hidden,
    input_norm_gain,
    query_weight,
    key_weight,
    value_weight,
    output_weight,
    query_bias_vector,
    value_bias_vector,
    adapter_down_maps,
    adapter_query_up,
    adapter_value_up,
    lengths,
    prompt_adapter,
):
    tp_width = lax.axis_size("tp")
    tp_place = lax.axis_index("tp")
    tok_rows = hidden.shape[0]
    group_tokens = tok_rows * tp_width
    rank_extent = adapter_query_up.shape[1]
    entry_slice = key_weight.shape[0]
    kv_heads = key_weight.shape[1]
    feat_slice = adapter_down_maps.shape[1]
    head_count = query_weight.shape[1] // HD

    down_flat = adapter_down_maps.reshape(1, -1)
    query_flat = adapter_query_up.reshape(1, -1)
    value_flat = adapter_value_up.reshape(1, -1)
    req_width = lax.axis_size("req")
    bank = ring_gather(
        jnp.concatenate([down_flat, query_flat, value_flat], axis=1)[0], "req", req_width
    )
    adapter_total = bank.shape[0]
    n_down, n_query = down_flat.shape[1], query_flat.shape[1]
    bank_down = bank[:, :n_down].reshape((adapter_total,) + adapter_down_maps.shape[1:])
    bank_query = bank[:, n_down : n_down + n_query].reshape(
        (adapter_total,) + adapter_query_up.shape[1:]
    )
    bank_value = bank[:, n_down + n_query :].reshape((adapter_total,) + adapter_value_up.shape[1:])

    prompt_length_list = lengths[0]
    adapter_choice_list = prompt_adapter[0]
    group_entry, segment, offset = prompt_layout(prompt_length_list, group_tokens)
    token_adapter = jnp.take(adapter_choice_list, segment)
    adapter_pick = token_adapter[:, None] == jnp.arange(adapter_total, dtype=jnp.int32)[None, :]

    gathered = ring_gather(hidden, "tp", tp_width).reshape(group_tokens, hidden.shape[1])
    normalized_input = rms_rows(gathered, input_norm_gain)

    own_features = lax.dynamic_slice_in_dim(
        normalized_input, tp_place * feat_slice, feat_slice, 1
    )
    terms = jnp.einsum(
        "tf,afr->tar", own_features, bank_down, preferred_element_type=jnp.float32
    )
    latent_part = jnp.sum(jnp.where(adapter_pick[:, :, None], terms, 0.0), axis=1)

    key_cols = jnp.einsum(
        "tm,ehm->the", normalized_input, key_weight, preferred_element_type=jnp.float32
    )
    value_cols = (
        jnp.einsum(
            "tm,ehm->the", normalized_input, value_weight, preferred_element_type=jnp.float32
        )
        + jnp.transpose(value_bias_vector)[None, :, :]
    )
    dest = jnp.arange(tp_width, dtype=jnp.int32)
    dest_head = dest * head_count // (HQ // HK)
    key_send = jnp.take(key_cols, dest_head, axis=1).transpose(1, 0, 2).reshape(tp_width, -1)
    value_send = jnp.take(value_cols, dest_head, axis=1).transpose(1, 0, 2).reshape(tp_width, -1)
    latent_send = jnp.broadcast_to(latent_part.reshape(1, -1), (tp_width, latent_part.size))
    up_send = (
        jnp.take(bank_value, dest_head, axis=3)
        .astype(jnp.float32)
        .transpose(3, 0, 1, 2)
        .reshape(tp_width, -1)
    )
    n_key, n_value, n_latent = key_send.shape[1], value_send.shape[1], latent_send.shape[1]
    received = source_order(
        ring_deliver(
            jnp.concatenate([key_send, value_send, latent_send, up_send], axis=1), "tp", tp_width
        ),
        "tp",
        tp_width,
    )
    key_head = (
        received[:, :n_key]
        .reshape(tp_width, group_tokens, entry_slice)
        .transpose(1, 0, 2)
        .reshape(group_tokens, HD)
        .astype(jnp.bfloat16)
    )
    value_base = (
        received[:, n_key : n_key + n_value]
        .reshape(tp_width, group_tokens, entry_slice)
        .transpose(1, 0, 2)
        .reshape(group_tokens, HD)
    )
    latent = (
        jnp.sum(
            received[:, n_key + n_value : n_key + n_value + n_latent].reshape(
                tp_width, group_tokens, 2 * rank_extent
            ),
            axis=0,
        )
        .astype(jnp.bfloat16)
    )
    value_up_head = (
        received[:, n_key + n_value + n_latent :]
        .reshape(tp_width, adapter_total, rank_extent, entry_slice)
        .transpose(1, 2, 0, 3)
        .reshape(adapter_total, rank_extent, HD)
    )

    pick = adapter_pick.astype(jnp.bfloat16)
    query_latent = (latent[:, None, :rank_extent] * pick[:, :, None]).reshape(group_tokens, -1)
    value_latent = (latent[:, None, rank_extent:] * pick[:, :, None]).reshape(group_tokens, -1)
    query_rows = (
        jnp.dot(normalized_input, query_weight, preferred_element_type=jnp.float32)
        + query_bias_vector
        + jnp.dot(
            query_latent,
            bank_query.reshape(-1, bank_query.shape[-1]),
            preferred_element_type=jnp.float32,
        )
    )
    value_head = (
        value_base
        + jnp.dot(
            value_latent,
            value_up_head.astype(jnp.bfloat16).reshape(-1, HD),
            preferred_element_type=jnp.float32,
        )
    ).astype(jnp.bfloat16)

    key_rot = rotate(key_head.astype(jnp.float32).reshape(group_tokens, 1, HD), offset)[
        :, 0, :
    ].astype(jnp.bfloat16)
    query_rot = rotate(query_rows.reshape(group_tokens, head_count, HD), offset).astype(
        jnp.bfloat16
    )
    mixed_heads = attend(query_rot, key_rot, value_head, segment).reshape(
        group_tokens, head_count * HD
    )
    block_terms = jnp.dot(mixed_heads, output_weight, preferred_element_type=jnp.float32).astype(
        jnp.bfloat16
    )
    owner_terms = ring_deliver(
        block_terms.reshape(tp_width, tok_rows, block_terms.shape[-1]), "tp", tp_width
    )
    projected = jnp.sum(owner_terms.astype(jnp.float32), axis=0)
    return (hidden.astype(jnp.float32) + projected).astype(jnp.bfloat16)


def solution(mesh):
    return jax.shard_map(
        shards,
        mesh=mesh,
        in_specs=(
            P(("req", "tp"), None),
            P(),
            P(None, "tp"),
            P("tp", None, None),
            P("tp", None, None),
            P("tp", None),
            P("tp"),
            P("tp", None),
            P("req", "tp", None),
            P("req", None, "tp"),
            P("req", None, "tp", None),
            P("req", None),
            P("req", None),
        ),
        out_specs=P(("req", "tp"), None),
        check_vma=False,
    )
```

```python
import jax
import jax.numpy as jnp
from jax import lax
from jax.sharding import PartitionSpec as P

HD = 128
HK = 8
HQ = 32


eps = 1e-06
rope_base = 1000000.0


def prompt_layout(prompt_length_list, group_tokens):
    ends = jnp.cumsum(prompt_length_list)
    starts = ends - prompt_length_list
    places = jnp.arange(group_tokens, dtype=jnp.int32)
    group_entry = (places[:, None] >= starts[None, :]) & (places[:, None] < ends[None, :])
    chosen = group_entry.astype(jnp.int32)
    segment = jnp.sum(
        chosen * jnp.arange(prompt_length_list.shape[0], dtype=jnp.int32)[None, :], axis=1
    )
    offset = places - jnp.sum(chosen * starts[None, :], axis=1)
    return (group_entry, segment, offset)


def rms_rows(source, input_norm_gain):
    values = source.astype(jnp.float32)
    return (
        values
        * lax.rsqrt(jnp.mean(values * values, axis=-1, keepdims=True) + eps)
        * input_norm_gain
    ).astype(jnp.bfloat16)


def rotate(values, offset):
    width = values.shape[-1]
    half_width = width // 2
    frequency = rope_base ** (-(jnp.arange(half_width, dtype=jnp.float32) * 2.0) / width)
    angles = offset.astype(jnp.float32)[:, None] * frequency[None, :]
    cosine = jnp.cos(angles)[:, None, :]
    sines = jnp.sin(angles)[:, None, :]
    lower_half = values[..., :half_width]
    upper_half = values[..., half_width:]
    return jnp.concatenate(
        [lower_half * cosine - upper_half * sines, upper_half * cosine + lower_half * sines],
        axis=-1,
    )


def attend(query_rot, key_rot, value_head, segment):
    scores = jnp.einsum(
        "qhd,kd->hqk", query_rot, key_rot, preferred_element_type=jnp.float32
    ) * HD ** (-0.5)
    places = jnp.arange(segment.shape[0], dtype=jnp.int32)
    allowed = (segment[:, None] == segment[None, :]) & (places[None, :] <= places[:, None])
    scores = jnp.where(allowed[None], scores, jnp.float32(-1e30))
    row_max = jnp.max(scores, axis=-1, keepdims=True)
    weights = jnp.exp(scores - row_max)
    probabilities = (weights / jnp.sum(weights, axis=-1, keepdims=True)).astype(jnp.bfloat16)
    mixed = jnp.einsum("hqk,kd->qhd", probabilities, value_head, preferred_element_type=jnp.float32)
    return mixed.astype(jnp.bfloat16)


def shards(
    hidden,
    input_norm_gain,
    query_weight,
    key_weight,
    value_weight,
    output_weight,
    query_bias_vector,
    value_bias_vector,
    adapter_down_maps,
    adapter_query_up,
    adapter_value_up,
    lengths,
    prompt_adapter,
):
    tp_width = lax.axis_size("tp")
    tp_place = lax.axis_index("tp")
    tok_rows = hidden.shape[0]
    group_tokens = tok_rows * tp_width
    rank_extent = adapter_query_up.shape[1]
    entry_slice = key_weight.shape[0]
    kv_heads = key_weight.shape[1]
    feat_slice = adapter_down_maps.shape[1]
    head_count = query_weight.shape[1] // HD

    down_flat = adapter_down_maps.reshape(1, -1)
    query_flat = adapter_query_up.reshape(1, -1)
    value_flat = adapter_value_up.reshape(1, -1)
    bank_piece = jnp.concatenate([down_flat, query_flat, value_flat], axis=1)
    req_width = lax.axis_size("req")
    bank = lax.all_to_all(
        jnp.broadcast_to(bank_piece, (req_width, bank_piece.shape[1])), "req", 0, 0, tiled=True
    )
    adapter_total = bank.shape[0]
    n_down, n_query = down_flat.shape[1], query_flat.shape[1]
    bank_down = bank[:, :n_down].reshape((adapter_total,) + adapter_down_maps.shape[1:])
    bank_query = bank[:, n_down : n_down + n_query].reshape(
        (adapter_total,) + adapter_query_up.shape[1:]
    )
    bank_value = bank[:, n_down + n_query :].reshape((adapter_total,) + adapter_value_up.shape[1:])

    prompt_length_list = lengths[0]
    adapter_choice_list = prompt_adapter[0]
    group_entry, segment, offset = prompt_layout(prompt_length_list, group_tokens)
    token_adapter = jnp.take(adapter_choice_list, segment)
    adapter_pick = token_adapter[:, None] == jnp.arange(adapter_total, dtype=jnp.int32)[None, :]

    gathered = lax.all_gather(hidden, "tp", axis=0, tiled=True)
    normalized_input = rms_rows(gathered, input_norm_gain)

    own_features = lax.dynamic_slice_in_dim(
        normalized_input, tp_place * feat_slice, feat_slice, 1
    )
    terms = jnp.einsum(
        "tf,afr->tar", own_features, bank_down, preferred_element_type=jnp.float32
    )
    latent_part = jnp.sum(jnp.where(adapter_pick[:, :, None], terms, 0.0), axis=1)

    key_cols = jnp.einsum(
        "tm,ehm->the", normalized_input, key_weight, preferred_element_type=jnp.float32
    )
    value_cols = (
        jnp.einsum(
            "tm,ehm->the", normalized_input, value_weight, preferred_element_type=jnp.float32
        )
        + jnp.transpose(value_bias_vector)[None, :, :]
    )
    dest = jnp.arange(tp_width, dtype=jnp.int32)
    dest_head = dest * head_count // (HQ // HK)
    key_send = jnp.take(key_cols, dest_head, axis=1).transpose(1, 0, 2).reshape(tp_width, -1)
    value_send = jnp.take(value_cols, dest_head, axis=1).transpose(1, 0, 2).reshape(tp_width, -1)
    latent_send = jnp.broadcast_to(latent_part.reshape(1, -1), (tp_width, latent_part.size))
    up_send = (
        jnp.take(bank_value, dest_head, axis=3)
        .astype(jnp.float32)
        .transpose(3, 0, 1, 2)
        .reshape(tp_width, -1)
    )
    n_key, n_value, n_latent = key_send.shape[1], value_send.shape[1], latent_send.shape[1]
    received = lax.all_to_all(
        jnp.concatenate([key_send, value_send, latent_send, up_send], axis=1),
        "tp",
        0,
        0,
        tiled=True,
    )
    key_head = (
        received[:, :n_key]
        .reshape(tp_width, group_tokens, entry_slice)
        .transpose(1, 0, 2)
        .reshape(group_tokens, HD)
        .astype(jnp.bfloat16)
    )
    value_base = (
        received[:, n_key : n_key + n_value]
        .reshape(tp_width, group_tokens, entry_slice)
        .transpose(1, 0, 2)
        .reshape(group_tokens, HD)
    )
    latent = (
        jnp.sum(
            received[:, n_key + n_value : n_key + n_value + n_latent].reshape(
                tp_width, group_tokens, 2 * rank_extent
            ),
            axis=0,
        )
        .astype(jnp.bfloat16)
    )
    value_up_head = (
        received[:, n_key + n_value + n_latent :]
        .reshape(tp_width, adapter_total, rank_extent, entry_slice)
        .transpose(1, 2, 0, 3)
        .reshape(adapter_total, rank_extent, HD)
    )

    pick = adapter_pick.astype(jnp.bfloat16)
    query_latent = (latent[:, None, :rank_extent] * pick[:, :, None]).reshape(group_tokens, -1)
    value_latent = (latent[:, None, rank_extent:] * pick[:, :, None]).reshape(group_tokens, -1)
    query_rows = (
        jnp.dot(normalized_input, query_weight, preferred_element_type=jnp.float32)
        + query_bias_vector
        + jnp.dot(
            query_latent,
            bank_query.reshape(-1, bank_query.shape[-1]),
            preferred_element_type=jnp.float32,
        )
    )
    value_head = (
        value_base
        + jnp.dot(
            value_latent,
            value_up_head.astype(jnp.bfloat16).reshape(-1, HD),
            preferred_element_type=jnp.float32,
        )
    ).astype(jnp.bfloat16)

    key_rot = rotate(key_head.astype(jnp.float32).reshape(group_tokens, 1, HD), offset)[
        :, 0, :
    ].astype(jnp.bfloat16)
    query_rot = rotate(query_rows.reshape(group_tokens, head_count, HD), offset).astype(
        jnp.bfloat16
    )
    mixed_heads = attend(query_rot, key_rot, value_head, segment).reshape(
        group_tokens, head_count * HD
    )
    block_terms = jnp.dot(mixed_heads, output_weight, preferred_element_type=jnp.float32).astype(
        jnp.bfloat16
    )
    owner_terms = lax.all_to_all(
        block_terms.reshape(tp_width, tok_rows, block_terms.shape[-1]), "tp", 0, 0, tiled=True
    )
    projected = jnp.sum(owner_terms.astype(jnp.float32), axis=0)
    return (hidden.astype(jnp.float32) + projected).astype(jnp.bfloat16)


def solution(mesh):
    return jax.shard_map(
        shards,
        mesh=mesh,
        in_specs=(
            P(("req", "tp"), None),
            P(),
            P(None, "tp"),
            P("tp", None, None),
            P("tp", None, None),
            P("tp", None),
            P("tp"),
            P("tp", None),
            P("req", "tp", None),
            P("req", None, "tp"),
            P("req", None, "tp", None),
            P("req", None),
            P("req", None),
        ),
        out_specs=P(("req", "tp"), None),
        check_vma=False,
    )
```

```python
import jax
import jax.numpy as jnp
from jax import lax
from jax.sharding import PartitionSpec as P

HD = 128
HK = 8
HQ = 32


eps = 1e-06
rope_base = 1000000.0


def prompt_layout(prompt_length_list, group_tokens):
    count = prompt_length_list.shape[0]
    prompts = jnp.arange(count, dtype=jnp.int32)
    ends = jnp.sum(
        jnp.where(prompts[None, :] <= prompts[:, None], prompt_length_list[None, :], 0), axis=1
    )
    starts = ends - prompt_length_list
    places = jnp.arange(group_tokens, dtype=jnp.int32)
    group_entry = (places[:, None] >= starts[None, :]) & (places[:, None] < ends[None, :])
    segment = jnp.sum(jnp.where(group_entry, prompts[None, :], 0), axis=1)
    offset = places - jnp.sum(jnp.where(group_entry, starts[None, :], 0), axis=1)
    return (group_entry, segment, offset)


def rms_rows(source, input_norm_gain):
    values = source.astype(jnp.float32)
    return (
        values
        * lax.rsqrt(jnp.mean(values * values, axis=-1, keepdims=True) + eps)
        * input_norm_gain
    ).astype(jnp.bfloat16)


def rotate(values, offset):
    width = values.shape[-1]
    half_width = width // 2
    frequency = rope_base ** (-(jnp.arange(half_width, dtype=jnp.float32) * 2.0) / width)
    angles = offset.astype(jnp.float32)[:, None] * frequency[None, :]
    cosine = jnp.cos(angles)[:, None, :]
    sines = jnp.sin(angles)[:, None, :]
    lower_half = values[..., :half_width]
    upper_half = values[..., half_width:]
    return jnp.concatenate(
        [lower_half * cosine - upper_half * sines, upper_half * cosine + lower_half * sines],
        axis=-1,
    )


def attend(query_rot, key_rot, value_head, segment):
    scores = jnp.einsum(
        "qhd,kd->hqk", query_rot, key_rot, preferred_element_type=jnp.float32
    ) * HD ** (-0.5)
    places = jnp.arange(segment.shape[0], dtype=jnp.int32)
    allowed = (segment[:, None] == segment[None, :]) & (places[None, :] <= places[:, None])
    scores = jnp.where(allowed[None], scores, jnp.float32(-1e30))
    row_max = jnp.max(scores, axis=-1, keepdims=True)
    weights = jnp.exp(scores - row_max)
    probabilities = (weights / jnp.sum(weights, axis=-1, keepdims=True)).astype(jnp.bfloat16)
    mixed = jnp.einsum("hqk,kd->qhd", probabilities, value_head, preferred_element_type=jnp.float32)
    return mixed.astype(jnp.bfloat16)


def shards(
    hidden,
    input_norm_gain,
    query_weight,
    key_weight,
    value_weight,
    output_weight,
    query_bias_vector,
    value_bias_vector,
    adapter_down_maps,
    adapter_query_up,
    adapter_value_up,
    lengths,
    prompt_adapter,
):
    tp_width = lax.axis_size("tp")
    tp_place = lax.axis_index("tp")
    tok_rows = hidden.shape[0]
    group_tokens = tok_rows * tp_width
    rank_extent = adapter_query_up.shape[1]
    entry_slice = key_weight.shape[0]
    kv_heads = key_weight.shape[1]
    feat_slice = adapter_down_maps.shape[1]
    head_count = query_weight.shape[1] // HD

    down_flat = adapter_down_maps.reshape(1, -1)
    query_flat = adapter_query_up.reshape(1, -1)
    value_flat = adapter_value_up.reshape(1, -1)
    bank_piece = jnp.concatenate([down_flat, query_flat, value_flat], axis=1)
    req_width = lax.axis_size("req")
    bank = lax.all_to_all(jnp.tile(bank_piece, (req_width, 1)), "req", 0, 0, tiled=True)
    adapter_total = bank.shape[0]
    n_down, n_query = down_flat.shape[1], query_flat.shape[1]
    bank_down = bank[:, :n_down].reshape((adapter_total,) + adapter_down_maps.shape[1:])
    bank_query = bank[:, n_down : n_down + n_query].reshape(
        (adapter_total,) + adapter_query_up.shape[1:]
    )
    bank_value = bank[:, n_down + n_query :].reshape((adapter_total,) + adapter_value_up.shape[1:])

    prompt_length_list = lengths[0]
    adapter_choice_list = prompt_adapter[0]
    group_entry, segment, offset = prompt_layout(prompt_length_list, group_tokens)
    token_adapter = jnp.sum(jnp.where(group_entry, adapter_choice_list[None, :], 0), axis=1)
    adapter_pick = token_adapter[:, None] == jnp.arange(adapter_total, dtype=jnp.int32)[None, :]

    gathered = lax.all_gather(hidden, "tp", axis=0, tiled=True)
    normalized_input = rms_rows(gathered, input_norm_gain)

    own_features = lax.dynamic_slice_in_dim(
        normalized_input, tp_place * feat_slice, feat_slice, 1
    )
    terms = jnp.dot(
        own_features,
        jnp.transpose(bank_down, (1, 0, 2)).reshape(feat_slice, -1),
        preferred_element_type=jnp.float32,
    ).reshape(group_tokens, adapter_total, 2 * rank_extent)
    latent_part = jnp.sum(jnp.where(adapter_pick[:, :, None], terms, 0.0), axis=1)

    key_cols = jnp.einsum(
        "tm,ehm->the", normalized_input, key_weight, preferred_element_type=jnp.float32
    )
    value_cols = (
        jnp.einsum(
            "tm,ehm->the", normalized_input, value_weight, preferred_element_type=jnp.float32
        )
        + jnp.transpose(value_bias_vector)[None, :, :]
    )
    per_kv = tp_width // kv_heads
    key_send = jnp.repeat(key_cols.transpose(1, 0, 2), per_kv, axis=0).reshape(tp_width, -1)
    value_send = jnp.repeat(value_cols.transpose(1, 0, 2), per_kv, axis=0).reshape(tp_width, -1)
    latent_send = jnp.broadcast_to(latent_part.reshape(1, -1), (tp_width, latent_part.size))
    up_send = jnp.repeat(
        bank_value.transpose(3, 0, 1, 2).reshape(kv_heads, -1).astype(jnp.float32), per_kv, axis=0
    )
    n_key, n_value, n_latent = key_send.shape[1], value_send.shape[1], latent_send.shape[1]
    received = lax.all_to_all(
        jnp.concatenate([key_send, value_send, latent_send, up_send], axis=1),
        "tp",
        0,
        0,
        tiled=True,
    )
    key_head = (
        received[:, :n_key]
        .reshape(tp_width, group_tokens, entry_slice)
        .transpose(1, 0, 2)
        .reshape(group_tokens, HD)
        .astype(jnp.bfloat16)
    )
    value_base = (
        received[:, n_key : n_key + n_value]
        .reshape(tp_width, group_tokens, entry_slice)
        .transpose(1, 0, 2)
        .reshape(group_tokens, HD)
    )
    latent = (
        jnp.sum(
            received[:, n_key + n_value : n_key + n_value + n_latent].reshape(
                tp_width, group_tokens, 2 * rank_extent
            ),
            axis=0,
        )
        .astype(jnp.bfloat16)
    )
    value_up_head = (
        received[:, n_key + n_value + n_latent :]
        .reshape(tp_width, adapter_total, rank_extent, entry_slice)
        .transpose(1, 2, 0, 3)
        .reshape(adapter_total, rank_extent, HD)
    )

    pick = adapter_pick.astype(jnp.bfloat16)
    query_latent = (latent[:, None, :rank_extent] * pick[:, :, None]).reshape(group_tokens, -1)
    value_latent = (latent[:, None, rank_extent:] * pick[:, :, None]).reshape(group_tokens, -1)
    query_rows = (
        jnp.dot(normalized_input, query_weight, preferred_element_type=jnp.float32)
        + query_bias_vector
        + jnp.dot(
            query_latent,
            bank_query.reshape(-1, bank_query.shape[-1]),
            preferred_element_type=jnp.float32,
        )
    )
    value_head = (
        value_base
        + jnp.dot(
            value_latent,
            value_up_head.astype(jnp.bfloat16).reshape(-1, HD),
            preferred_element_type=jnp.float32,
        )
    ).astype(jnp.bfloat16)

    key_rot = rotate(key_head.astype(jnp.float32).reshape(group_tokens, 1, HD), offset)[
        :, 0, :
    ].astype(jnp.bfloat16)
    query_rot = rotate(query_rows.reshape(group_tokens, head_count, HD), offset).astype(
        jnp.bfloat16
    )
    mixed_heads = attend(query_rot, key_rot, value_head, segment).reshape(
        group_tokens, head_count * HD
    )
    block_terms = jnp.dot(mixed_heads, output_weight, preferred_element_type=jnp.float32).astype(
        jnp.bfloat16
    )
    owner_terms = lax.all_to_all(
        block_terms.reshape(tp_width, tok_rows, block_terms.shape[-1]), "tp", 0, 0, tiled=True
    )
    projected = jnp.sum(owner_terms.astype(jnp.float32), axis=0)
    return (hidden.astype(jnp.float32) + projected).astype(jnp.bfloat16)


def solution(mesh):
    return jax.shard_map(
        shards,
        mesh=mesh,
        in_specs=(
            P(("req", "tp"), None),
            P(),
            P(None, "tp"),
            P("tp", None, None),
            P("tp", None, None),
            P("tp", None),
            P("tp"),
            P("tp", None),
            P("req", "tp", None),
            P("req", None, "tp"),
            P("req", None, "tp", None),
            P("req", None),
            P("req", None),
        ),
        out_specs=P(("req", "tp"), None),
        check_vma=False,
    )
```

```python
import jax
import jax.numpy as jnp
from jax import lax
from jax.sharding import PartitionSpec as P

HD = 128
HK = 8
HQ = 32


eps = 1e-06
rope_base = 1000000.0


def prompt_layout(prompt_length_list, group_tokens):
    count = prompt_length_list.shape[0]
    prompts = jnp.arange(count, dtype=jnp.int32)
    ends = jnp.sum(
        jnp.where(prompts[None, :] <= prompts[:, None], prompt_length_list[None, :], 0), axis=1
    )
    starts = ends - prompt_length_list
    places = jnp.arange(group_tokens, dtype=jnp.int32)
    group_entry = (places[:, None] >= starts[None, :]) & (places[:, None] < ends[None, :])
    segment = jnp.sum(jnp.where(group_entry, prompts[None, :], 0), axis=1)
    offset = places - jnp.sum(jnp.where(group_entry, starts[None, :], 0), axis=1)
    return (group_entry, segment, offset)


def rms_rows(source, input_norm_gain):
    values = source.astype(jnp.float32)
    return (
        values
        * lax.rsqrt(jnp.mean(values * values, axis=-1, keepdims=True) + eps)
        * input_norm_gain
    ).astype(jnp.bfloat16)


def rotate(values, offset):
    width = values.shape[-1]
    half_width = width // 2
    frequency = rope_base ** (-(jnp.arange(half_width, dtype=jnp.float32) * 2.0) / width)
    angles = offset.astype(jnp.float32)[:, None] * frequency[None, :]
    cosine = jnp.cos(angles)[:, None, :]
    sines = jnp.sin(angles)[:, None, :]
    lower_half = values[..., :half_width]
    upper_half = values[..., half_width:]
    return jnp.concatenate(
        [lower_half * cosine - upper_half * sines, upper_half * cosine + lower_half * sines],
        axis=-1,
    )


def attend(query_rot, key_rot, value_head, segment):
    scores = jnp.einsum(
        "qhd,kd->hqk", query_rot, key_rot, preferred_element_type=jnp.float32
    ) * HD ** (-0.5)
    places = jnp.arange(segment.shape[0], dtype=jnp.int32)
    allowed = (segment[:, None] == segment[None, :]) & (places[None, :] <= places[:, None])
    scores = jnp.where(allowed[None], scores, jnp.float32(-1e30))
    row_max = jnp.max(scores, axis=-1, keepdims=True)
    weights = jnp.exp(scores - row_max)
    probabilities = (weights / jnp.sum(weights, axis=-1, keepdims=True)).astype(jnp.bfloat16)
    mixed = jnp.einsum("hqk,kd->qhd", probabilities, value_head, preferred_element_type=jnp.float32)
    return mixed.astype(jnp.bfloat16)


def shards(
    hidden,
    input_norm_gain,
    query_weight,
    key_weight,
    value_weight,
    output_weight,
    query_bias_vector,
    value_bias_vector,
    adapter_down_maps,
    adapter_query_up,
    adapter_value_up,
    lengths,
    prompt_adapter,
):
    tp_width = lax.axis_size("tp")
    tp_place = lax.axis_index("tp")
    tok_rows = hidden.shape[0]
    group_tokens = tok_rows * tp_width
    rank_extent = adapter_query_up.shape[1]
    entry_slice = key_weight.shape[0]
    kv_heads = key_weight.shape[1]
    feat_slice = adapter_down_maps.shape[1]
    head_count = query_weight.shape[1] // HD

    down_flat = adapter_down_maps.reshape(1, -1)
    query_flat = adapter_query_up.reshape(1, -1)
    value_flat = adapter_value_up.reshape(1, -1)
    bank_piece = jnp.concatenate([down_flat, query_flat, value_flat], axis=1)
    req_width = lax.axis_size("req")
    bank = lax.all_to_all(jnp.tile(bank_piece, (req_width, 1)), "req", 0, 0, tiled=True)
    adapter_total = bank.shape[0]
    n_down, n_query = down_flat.shape[1], query_flat.shape[1]
    bank_down = bank[:, :n_down].reshape((adapter_total,) + adapter_down_maps.shape[1:])
    bank_query = bank[:, n_down : n_down + n_query].reshape(
        (adapter_total,) + adapter_query_up.shape[1:]
    )
    bank_value = bank[:, n_down + n_query :].reshape((adapter_total,) + adapter_value_up.shape[1:])

    prompt_length_list = lengths[0]
    adapter_choice_list = prompt_adapter[0]
    group_entry, segment, offset = prompt_layout(prompt_length_list, group_tokens)
    token_adapter = jnp.sum(jnp.where(group_entry, adapter_choice_list[None, :], 0), axis=1)
    adapter_pick = token_adapter[:, None] == jnp.arange(adapter_total, dtype=jnp.int32)[None, :]

    gathered = lax.all_gather(hidden, "tp", axis=0, tiled=True)
    normalized_input = rms_rows(gathered, input_norm_gain)

    own_features = lax.dynamic_slice_in_dim(
        normalized_input, tp_place * feat_slice, feat_slice, 1
    )
    terms = jnp.dot(
        own_features,
        jnp.transpose(bank_down, (1, 0, 2)).reshape(feat_slice, -1),
        preferred_element_type=jnp.float32,
    ).reshape(group_tokens, adapter_total, 2 * rank_extent)
    latent_part = jnp.sum(jnp.where(adapter_pick[:, :, None], terms, 0.0), axis=1)

    key_cols = jnp.einsum(
        "tm,ehm->the", normalized_input, key_weight, preferred_element_type=jnp.float32
    )
    value_cols = (
        jnp.einsum(
            "tm,ehm->the", normalized_input, value_weight, preferred_element_type=jnp.float32
        )
        + jnp.transpose(value_bias_vector)[None, :, :]
    )
    per_kv = tp_width // kv_heads
    key_send = jnp.repeat(key_cols.transpose(1, 0, 2), per_kv, axis=0).reshape(tp_width, -1)
    value_send = jnp.repeat(value_cols.transpose(1, 0, 2), per_kv, axis=0).reshape(tp_width, -1)
    latent_send = jnp.broadcast_to(latent_part.reshape(1, -1), (tp_width, latent_part.size))
    up_send = jnp.repeat(
        bank_value.transpose(3, 0, 1, 2).reshape(kv_heads, -1).astype(jnp.float32), per_kv, axis=0
    )
    n_key, n_value, n_latent = key_send.shape[1], value_send.shape[1], latent_send.shape[1]
    kv_send = jnp.concatenate([key_send, value_send, latent_send, up_send], axis=1)
    kv_width = kv_send.shape[1]
    kv_pad = (-kv_width) % (8 * 128)
    kv_send = jnp.pad(kv_send, ((0, 0), (0, kv_pad))).reshape(tp_width, -1, 128)
    received = lax.all_to_all(kv_send, "tp", 0, 0, tiled=True).reshape(tp_width, -1)[:, :kv_width]
    key_head = (
        received[:, :n_key]
        .reshape(tp_width, group_tokens, entry_slice)
        .transpose(1, 0, 2)
        .reshape(group_tokens, HD)
        .astype(jnp.bfloat16)
    )
    value_base = (
        received[:, n_key : n_key + n_value]
        .reshape(tp_width, group_tokens, entry_slice)
        .transpose(1, 0, 2)
        .reshape(group_tokens, HD)
    )
    latent = (
        jnp.sum(
            received[:, n_key + n_value : n_key + n_value + n_latent].reshape(
                tp_width, group_tokens, 2 * rank_extent
            ),
            axis=0,
        )
        .astype(jnp.bfloat16)
    )
    value_up_head = (
        received[:, n_key + n_value + n_latent :]
        .reshape(tp_width, adapter_total, rank_extent, entry_slice)
        .transpose(1, 2, 0, 3)
        .reshape(adapter_total, rank_extent, HD)
    )

    pick = adapter_pick.astype(jnp.bfloat16)
    query_latent = (latent[:, None, :rank_extent] * pick[:, :, None]).reshape(group_tokens, -1)
    value_latent = (latent[:, None, rank_extent:] * pick[:, :, None]).reshape(group_tokens, -1)
    query_rows = (
        jnp.dot(normalized_input, query_weight, preferred_element_type=jnp.float32)
        + query_bias_vector
        + jnp.dot(
            query_latent,
            bank_query.reshape(-1, bank_query.shape[-1]),
            preferred_element_type=jnp.float32,
        )
    )
    value_head = (
        value_base
        + jnp.dot(
            value_latent,
            value_up_head.astype(jnp.bfloat16).reshape(-1, HD),
            preferred_element_type=jnp.float32,
        )
    ).astype(jnp.bfloat16)

    key_rot = rotate(key_head.astype(jnp.float32).reshape(group_tokens, 1, HD), offset)[
        :, 0, :
    ].astype(jnp.bfloat16)
    query_rot = rotate(query_rows.reshape(group_tokens, head_count, HD), offset).astype(
        jnp.bfloat16
    )
    mixed_heads = attend(query_rot, key_rot, value_head, segment).reshape(
        group_tokens, head_count * HD
    )
    block_terms = jnp.dot(mixed_heads, output_weight, preferred_element_type=jnp.float32).astype(
        jnp.bfloat16
    )
    owner_terms = lax.all_to_all(
        block_terms.reshape(tp_width, tok_rows, block_terms.shape[-1]), "tp", 0, 0, tiled=True
    )
    projected = jnp.sum(owner_terms.astype(jnp.float32), axis=0)
    return (hidden.astype(jnp.float32) + projected).astype(jnp.bfloat16)


def solution(mesh):
    return jax.shard_map(
        shards,
        mesh=mesh,
        in_specs=(
            P(("req", "tp"), None),
            P(),
            P(None, "tp"),
            P("tp", None, None),
            P("tp", None, None),
            P("tp", None),
            P("tp"),
            P("tp", None),
            P("req", "tp", None),
            P("req", None, "tp"),
            P("req", None, "tp", None),
            P("req", None),
            P("req", None),
        ),
        out_specs=P(("req", "tp"), None),
        check_vma=False,
    )
```

```python
import jax
import jax.numpy as jnp
from jax import lax
from jax.sharding import PartitionSpec as P

HD = 128
HK = 8
HQ = 32


eps = 1e-06
rope_base = 1000000.0


def prompt_layout(prompt_length_list, group_tokens):
    count = prompt_length_list.shape[0]
    prompts = jnp.arange(count, dtype=jnp.int32)
    ends = jnp.sum(
        jnp.where(prompts[None, :] <= prompts[:, None], prompt_length_list[None, :], 0), axis=1
    )
    starts = ends - prompt_length_list
    places = jnp.arange(group_tokens, dtype=jnp.int32)
    group_entry = (places[:, None] >= starts[None, :]) & (places[:, None] < ends[None, :])
    segment = jnp.sum(jnp.where(group_entry, prompts[None, :], 0), axis=1)
    offset = places - jnp.sum(jnp.where(group_entry, starts[None, :], 0), axis=1)
    return (group_entry, segment, offset)


def rms_rows(source, input_norm_gain):
    values = source.astype(jnp.float32)
    return (
        values
        * lax.rsqrt(jnp.mean(values * values, axis=-1, keepdims=True) + eps)
        * input_norm_gain
    ).astype(jnp.bfloat16)


def rotate(values, offset):
    width = values.shape[-1]
    half_width = width // 2
    frequency = rope_base ** (-(jnp.arange(half_width, dtype=jnp.float32) * 2.0) / width)
    angles = offset.astype(jnp.float32)[:, None] * frequency[None, :]
    cosine = jnp.cos(angles)[:, None, :]
    sines = jnp.sin(angles)[:, None, :]
    lower_half = values[..., :half_width]
    upper_half = values[..., half_width:]
    return jnp.concatenate(
        [lower_half * cosine - upper_half * sines, upper_half * cosine + lower_half * sines],
        axis=-1,
    )


def rotate_rows(values_t, offset):
    width = values_t.shape[0]
    half_width = width // 2
    frequency = rope_base ** (-(jnp.arange(half_width, dtype=jnp.float32) * 2.0) / width)
    angles = offset.astype(jnp.float32)[None, :] * frequency[:, None]
    cosine = jnp.cos(angles)
    sines = jnp.sin(angles)
    lower_half = values_t[:half_width]
    upper_half = values_t[half_width:]
    return jnp.concatenate(
        [lower_half * cosine - upper_half * sines, upper_half * cosine + lower_half * sines],
        axis=0,
    )


def attend(query_rot, key_rot_t, value_head_t, segment):
    scores = jnp.einsum(
        "qhd,dk->hqk", query_rot, key_rot_t, preferred_element_type=jnp.float32
    ) * HD ** (-0.5)
    places = jnp.arange(segment.shape[0], dtype=jnp.int32)
    allowed = (segment[:, None] == segment[None, :]) & (places[None, :] <= places[:, None])
    scores = jnp.where(allowed[None], scores, jnp.float32(-1e30))
    row_max = jnp.max(scores, axis=-1, keepdims=True)
    weights = jnp.exp(scores - row_max)
    probabilities = (weights / jnp.sum(weights, axis=-1, keepdims=True)).astype(jnp.bfloat16)
    mixed = jnp.einsum(
        "hqk,dk->qhd", probabilities, value_head_t, preferred_element_type=jnp.float32
    )
    return mixed.astype(jnp.bfloat16)


def shards(
    hidden,
    input_norm_gain,
    query_weight,
    key_weight,
    value_weight,
    output_weight,
    query_bias_vector,
    value_bias_vector,
    adapter_down_maps,
    adapter_query_up,
    adapter_value_up,
    lengths,
    prompt_adapter,
):
    tp_width = lax.axis_size("tp")
    tp_place = lax.axis_index("tp")
    tok_rows = hidden.shape[0]
    group_tokens = tok_rows * tp_width
    rank_extent = adapter_query_up.shape[1]
    entry_slice = key_weight.shape[0]
    kv_heads = key_weight.shape[1]
    feat_slice = adapter_down_maps.shape[1]
    head_count = query_weight.shape[1] // HD

    down_flat = adapter_down_maps.reshape(1, -1)
    query_flat = adapter_query_up.reshape(1, -1)
    value_flat = adapter_value_up.reshape(1, -1)
    bank_piece = jnp.concatenate([down_flat, query_flat, value_flat], axis=1)
    req_width = lax.axis_size("req")
    bank = lax.all_to_all(jnp.tile(bank_piece, (req_width, 1)), "req", 0, 0, tiled=True)
    adapter_total = bank.shape[0]
    n_down, n_query = down_flat.shape[1], query_flat.shape[1]
    bank_down = bank[:, :n_down].reshape((adapter_total,) + adapter_down_maps.shape[1:])
    bank_query = bank[:, n_down : n_down + n_query].reshape(
        (adapter_total,) + adapter_query_up.shape[1:]
    )
    bank_value = bank[:, n_down + n_query :].reshape((adapter_total,) + adapter_value_up.shape[1:])

    prompt_length_list = lengths[0]
    adapter_choice_list = prompt_adapter[0]
    group_entry, segment, offset = prompt_layout(prompt_length_list, group_tokens)
    token_adapter = jnp.sum(jnp.where(group_entry, adapter_choice_list[None, :], 0), axis=1)
    adapter_pick = token_adapter[:, None] == jnp.arange(adapter_total, dtype=jnp.int32)[None, :]

    gathered = lax.all_gather(hidden, "tp", axis=0, tiled=True)
    normalized_input = rms_rows(gathered, input_norm_gain)

    own_features = lax.dynamic_slice_in_dim(
        normalized_input, tp_place * feat_slice, feat_slice, 1
    )
    terms = jnp.dot(
        own_features,
        jnp.transpose(bank_down, (1, 0, 2)).reshape(feat_slice, -1),
        preferred_element_type=jnp.float32,
    ).reshape(group_tokens, adapter_total, 2 * rank_extent)
    latent_part = jnp.sum(jnp.where(adapter_pick[:, :, None], terms, 0.0), axis=1)

    key_cols = jnp.einsum(
        "tm,ehm->het", normalized_input, key_weight, preferred_element_type=jnp.float32
    )
    value_cols = (
        jnp.einsum(
            "tm,ehm->het", normalized_input, value_weight, preferred_element_type=jnp.float32
        )
        + jnp.transpose(value_bias_vector)[:, :, None]
    )
    per_kv = tp_width // kv_heads
    key_send = jnp.repeat(key_cols, per_kv, axis=0).reshape(tp_width, -1)
    value_send = jnp.repeat(value_cols, per_kv, axis=0).reshape(tp_width, -1)
    latent_send = jnp.broadcast_to(latent_part.reshape(1, -1), (tp_width, latent_part.size))
    up_send = jnp.repeat(
        bank_value.transpose(3, 0, 1, 2).reshape(kv_heads, -1).astype(jnp.float32), per_kv, axis=0
    )
    n_key, n_value, n_latent = key_send.shape[1], value_send.shape[1], latent_send.shape[1]
    kv_send = jnp.concatenate([key_send, value_send, latent_send, up_send], axis=1)
    kv_width = kv_send.shape[1]
    kv_pad = (-kv_width) % (8 * 128)
    kv_send = jnp.pad(kv_send, ((0, 0), (0, kv_pad))).reshape(tp_width, -1, 128)
    received = lax.all_to_all(kv_send, "tp", 0, 0, tiled=True).reshape(tp_width, -1)[:, :kv_width]
    key_head_t = received[:, :n_key].reshape(HD, group_tokens).astype(jnp.bfloat16)
    value_base_t = received[:, n_key : n_key + n_value].reshape(HD, group_tokens)
    latent = (
        jnp.sum(
            received[:, n_key + n_value : n_key + n_value + n_latent].reshape(
                tp_width, group_tokens, 2 * rank_extent
            ),
            axis=0,
        )
        .astype(jnp.bfloat16)
    )
    value_up_head = (
        received[:, n_key + n_value + n_latent :]
        .reshape(tp_width, adapter_total, rank_extent, entry_slice)
        .transpose(1, 2, 0, 3)
        .reshape(adapter_total, rank_extent, HD)
    )

    pick = adapter_pick.astype(jnp.bfloat16)
    query_latent = (latent[:, None, :rank_extent] * pick[:, :, None]).reshape(group_tokens, -1)
    value_latent = (latent[:, None, rank_extent:] * pick[:, :, None]).reshape(group_tokens, -1)
    query_rows = (
        jnp.dot(normalized_input, query_weight, preferred_element_type=jnp.float32)
        + query_bias_vector
        + jnp.dot(
            query_latent,
            bank_query.reshape(-1, bank_query.shape[-1]),
            preferred_element_type=jnp.float32,
        )
    )
    value_head_t = (
        value_base_t
        + jnp.einsum(
            "ta,ae->et",
            value_latent,
            value_up_head.astype(jnp.bfloat16).reshape(-1, HD),
            preferred_element_type=jnp.float32,
        )
    ).astype(jnp.bfloat16)

    key_rot_t = rotate_rows(key_head_t.astype(jnp.float32), offset).astype(jnp.bfloat16)
    query_rot = rotate(query_rows.reshape(group_tokens, head_count, HD), offset).astype(
        jnp.bfloat16
    )
    mixed_heads = attend(query_rot, key_rot_t, value_head_t, segment).reshape(
        group_tokens, head_count * HD
    )
    block_terms = jnp.dot(mixed_heads, output_weight, preferred_element_type=jnp.float32).astype(
        jnp.bfloat16
    )
    owner_terms = lax.all_to_all(
        block_terms.reshape(tp_width, tok_rows, block_terms.shape[-1]), "tp", 0, 0, tiled=True
    )
    projected = jnp.sum(owner_terms.astype(jnp.float32), axis=0)
    return (hidden.astype(jnp.float32) + projected).astype(jnp.bfloat16)


def solution(mesh):
    return jax.shard_map(
        shards,
        mesh=mesh,
        in_specs=(
            P(("req", "tp"), None),
            P(),
            P(None, "tp"),
            P("tp", None, None),
            P("tp", None, None),
            P("tp", None),
            P("tp"),
            P("tp", None),
            P("req", "tp", None),
            P("req", None, "tp"),
            P("req", None, "tp", None),
            P("req", None),
            P("req", None),
        ),
        out_specs=P(("req", "tp"), None),
        check_vma=False,
    )
```

```python
import jax
import jax.numpy as jnp
from jax import lax
from jax.sharding import PartitionSpec as P

HD = 128
HK = 8
HQ = 32


eps = 1e-06
rope_base = 1000000.0


def prompt_layout(prompt_length_list, group_tokens):
    count = prompt_length_list.shape[0]
    prompts = jnp.arange(count, dtype=jnp.int32)
    ends = jnp.sum(
        jnp.where(prompts[None, :] <= prompts[:, None], prompt_length_list[None, :], 0), axis=1
    )
    starts = ends - prompt_length_list
    places = jnp.arange(group_tokens, dtype=jnp.int32)
    group_entry = (places[:, None] >= starts[None, :]) & (places[:, None] < ends[None, :])
    segment = jnp.sum(jnp.where(group_entry, prompts[None, :], 0), axis=1)
    offset = places - jnp.sum(jnp.where(group_entry, starts[None, :], 0), axis=1)
    return (group_entry, segment, offset)


def rms_rows(source, input_norm_gain):
    values = source.astype(jnp.float32)
    return (
        values
        * lax.rsqrt(jnp.mean(values * values, axis=-1, keepdims=True) + eps)
        * input_norm_gain
    ).astype(jnp.bfloat16)


def rotate(values, offset):
    width = values.shape[-1]
    half_width = width // 2
    frequency = rope_base ** (-(jnp.arange(half_width, dtype=jnp.float32) * 2.0) / width)
    angles = offset.astype(jnp.float32)[:, None] * frequency[None, :]
    cosine = jnp.cos(angles)[:, None, :]
    sines = jnp.sin(angles)[:, None, :]
    lower_half = values[..., :half_width]
    upper_half = values[..., half_width:]
    return jnp.concatenate(
        [lower_half * cosine - upper_half * sines, upper_half * cosine + lower_half * sines],
        axis=-1,
    )


def rotate_rows(values_t, offset):
    width = values_t.shape[0]
    half_width = width // 2
    frequency = rope_base ** (-(jnp.arange(half_width, dtype=jnp.float32) * 2.0) / width)
    angles = offset.astype(jnp.float32)[None, :] * frequency[:, None]
    cosine = jnp.cos(angles)
    sines = jnp.sin(angles)
    lower_half = values_t[:half_width]
    upper_half = values_t[half_width:]
    return jnp.concatenate(
        [lower_half * cosine - upper_half * sines, upper_half * cosine + lower_half * sines],
        axis=0,
    )


def attend(query_rot, key_rot_t, value_head_t, segment):
    scores = jnp.einsum(
        "qhd,dk->hqk", query_rot, key_rot_t, preferred_element_type=jnp.float32
    ) * HD ** (-0.5)
    places = jnp.arange(segment.shape[0], dtype=jnp.int32)
    allowed = (segment[:, None] == segment[None, :]) & (places[None, :] <= places[:, None])
    scores = jnp.where(allowed[None], scores, jnp.float32(-1e30))
    row_max = jnp.max(scores, axis=-1, keepdims=True)
    weights = jnp.exp(scores - row_max)
    probabilities = (weights / jnp.sum(weights, axis=-1, keepdims=True)).astype(jnp.bfloat16)
    mixed = jnp.einsum(
        "hqk,dk->qhd", probabilities, value_head_t, preferred_element_type=jnp.float32
    )
    return mixed.astype(jnp.bfloat16)


def shards(
    hidden,
    input_norm_gain,
    query_weight,
    key_weight,
    value_weight,
    output_weight,
    query_bias_vector,
    value_bias_vector,
    adapter_down_maps,
    adapter_query_up,
    adapter_value_up,
    lengths,
    prompt_adapter,
):
    tp_width = lax.axis_size("tp")
    tp_place = lax.axis_index("tp")
    tok_rows = hidden.shape[0]
    group_tokens = tok_rows * tp_width
    rank_extent = adapter_query_up.shape[1]
    entry_slice = key_weight.shape[0]
    kv_heads = key_weight.shape[1]
    feat_slice = adapter_down_maps.shape[1]
    head_count = query_weight.shape[1] // HD

    down_flat = adapter_down_maps.reshape(1, -1)
    query_flat = adapter_query_up.reshape(1, -1)
    value_flat = adapter_value_up.reshape(1, -1)
    bank_piece = jnp.concatenate([down_flat, query_flat, value_flat], axis=1)
    req_width = lax.axis_size("req")
    bank = lax.all_to_all(jnp.tile(bank_piece, (req_width, 1)), "req", 0, 0, tiled=True)
    adapter_total = bank.shape[0]
    n_down, n_query = down_flat.shape[1], query_flat.shape[1]
    bank_down = bank[:, :n_down].reshape((adapter_total,) + adapter_down_maps.shape[1:])
    bank_query = bank[:, n_down : n_down + n_query].reshape(
        (adapter_total,) + adapter_query_up.shape[1:]
    )
    bank_value = bank[:, n_down + n_query :].reshape((adapter_total,) + adapter_value_up.shape[1:])

    prompt_length_list = lengths[0]
    adapter_choice_list = prompt_adapter[0]
    group_entry, segment, offset = prompt_layout(prompt_length_list, group_tokens)
    token_adapter = jnp.sum(jnp.where(group_entry, adapter_choice_list[None, :], 0), axis=1)
    adapter_pick = token_adapter[:, None] == jnp.arange(adapter_total, dtype=jnp.int32)[None, :]

    gathered = lax.all_gather(hidden, "tp", axis=0, tiled=True)
    normalized_input = rms_rows(gathered, input_norm_gain)

    own_features = lax.dynamic_slice_in_dim(
        normalized_input, tp_place * feat_slice, feat_slice, 1
    )
    terms = jnp.dot(
        own_features,
        jnp.transpose(bank_down, (1, 0, 2)).reshape(feat_slice, -1),
        preferred_element_type=jnp.float32,
    ).reshape(group_tokens, adapter_total, 2 * rank_extent)
    latent_part = jnp.sum(jnp.where(adapter_pick[:, :, None], terms, 0.0), axis=1)

    key_cols = jnp.einsum(
        "tm,ehm->het", normalized_input, key_weight, preferred_element_type=jnp.float32
    )
    value_cols = (
        jnp.einsum(
            "tm,ehm->het", normalized_input, value_weight, preferred_element_type=jnp.float32
        )
        + jnp.transpose(value_bias_vector)[:, :, None]
    )
    per_kv = tp_width // kv_heads
    key_send = jnp.repeat(key_cols, per_kv, axis=0).reshape(tp_width, -1)
    value_send = jnp.repeat(value_cols, per_kv, axis=0).reshape(tp_width, -1)
    latent_send = jnp.broadcast_to(latent_part.reshape(1, -1), (tp_width, latent_part.size))
    up_send = jnp.repeat(
        bank_value.transpose(3, 0, 1, 2).reshape(kv_heads, -1).astype(jnp.float32), per_kv, axis=0
    )
    n_key, n_value, n_latent = key_send.shape[1], value_send.shape[1], latent_send.shape[1]
    kv_send = jnp.concatenate([key_send, value_send, latent_send, up_send], axis=1)
    kv_width = kv_send.shape[1]
    kv_pad = (-kv_width) % (8 * 128)
    kv_send = jnp.pad(kv_send, ((0, 0), (0, kv_pad))).reshape(tp_width, -1, 128)
    received = lax.all_to_all(kv_send, "tp", 0, 0, tiled=True).reshape(tp_width, -1)[:, :kv_width]
    key_head_t = received[:, :n_key].reshape(HD, group_tokens).astype(jnp.bfloat16)
    value_base_t = received[:, n_key : n_key + n_value].reshape(HD, group_tokens)
    latent = (
        jnp.sum(
            received[:, n_key + n_value : n_key + n_value + n_latent].reshape(
                tp_width, group_tokens, 2 * rank_extent
            ),
            axis=0,
        )
        .astype(jnp.bfloat16)
    )
    value_up_rows = received[:, n_key + n_value + n_latent :].reshape(
        tp_width, adapter_total * rank_extent, entry_slice
    )

    pick = adapter_pick.astype(jnp.bfloat16)
    query_latent = (latent[:, None, :rank_extent] * pick[:, :, None]).reshape(group_tokens, -1)
    value_latent = (latent[:, None, rank_extent:] * pick[:, :, None]).reshape(group_tokens, -1)
    query_rows = (
        jnp.dot(normalized_input, query_weight, preferred_element_type=jnp.float32)
        + query_bias_vector
        + jnp.dot(
            query_latent,
            bank_query.reshape(-1, bank_query.shape[-1]),
            preferred_element_type=jnp.float32,
        )
    )
    value_head_t = (
        value_base_t
        + jnp.einsum(
            "ta,sae->set",
            value_latent,
            value_up_rows.astype(jnp.bfloat16),
            preferred_element_type=jnp.float32,
        ).reshape(HD, group_tokens)
    ).astype(jnp.bfloat16)

    key_rot_t = rotate_rows(key_head_t.astype(jnp.float32), offset).astype(jnp.bfloat16)
    query_rot = rotate(query_rows.reshape(group_tokens, head_count, HD), offset).astype(
        jnp.bfloat16
    )
    mixed_heads = attend(query_rot, key_rot_t, value_head_t, segment).reshape(
        group_tokens, head_count * HD
    )
    block_terms = jnp.dot(mixed_heads, output_weight, preferred_element_type=jnp.float32).astype(
        jnp.bfloat16
    )
    owner_terms = lax.all_to_all(
        block_terms.reshape(tp_width, tok_rows, block_terms.shape[-1]), "tp", 0, 0, tiled=True
    )
    projected = jnp.sum(owner_terms.astype(jnp.float32), axis=0)
    return (hidden.astype(jnp.float32) + projected).astype(jnp.bfloat16)


def solution(mesh):
    return jax.shard_map(
        shards,
        mesh=mesh,
        in_specs=(
            P(("req", "tp"), None),
            P(),
            P(None, "tp"),
            P("tp", None, None),
            P("tp", None, None),
            P("tp", None),
            P("tp"),
            P("tp", None),
            P("req", "tp", None),
            P("req", None, "tp"),
            P("req", None, "tp", None),
            P("req", None),
            P("req", None),
        ),
        out_specs=P(("req", "tp"), None),
        check_vma=False,
    )
```
